1024 devices in a mesh: layer: 4 (over z_hi, core), blk: 256 (over z_lo, y, x).
Axes of the slice: x: 8, y: 8, z: 8 (z_hi: 2, z_lo: 4; z = z_hi * 4 + z_lo), core: 2. Of those that a mesh axis runs over, the one named last changes fastest.
Arguments:
- density: float32 [768, 6, 256, 256], P('blk'), may hold values from -0.15625 to 0.15625
- pattern: int32 [768, 6], replicated, may hold values from 0 to 767, as said below
Outputs:
- squared: float32 [768, 6, 256, 256], P('blk', None, None, 'layer')
- purified: float32 [768, 6, 256, 256], P('blk', None, None, 'layer')
The draws below stay inside these ranges and needn't reach their ends.
Inputs may be any that keep to these rules, and one draw needn't show every extreme that they name: pattern[i, 0] = i and pattern[i, 1 .. 5] = (i + d) mod 768 for 5 distinct nonzero offsets d in -3 .. 3.
All inputs are finite; a program needn't handle non-finite values.
Results may differ from the reference program's by a relative error of at most 0.0016.
Values may be sent and summed in bfloat16 or wider, within the bound.
No kernel may reach another device: no remote copies, remote signals or barrier semaphores. Data moves between devices by JAX's collectives and lax.ppermute only.
A program may use at most 64 MiB of HBM per device.

```python
import jax
import jax.numpy as jnp
from jax import lax

BS = 256
K = 6
BAND = 3
NB = 768


def draw_pattern(key, part):
    rows = jnp.arange(NB, dtype=jnp.int32)
    dropped = jax.random.randint(key, (NB,), 0, 2 * BAND, dtype=jnp.int32)
    nonzero = jnp.concatenate([jnp.arange(-BAND, 0, dtype=jnp.int32), jnp.arange(1, BAND + 1, dtype=jnp.int32)])
    places = jnp.arange(K - 1, dtype=jnp.int32)
    index = places[None, :] + (places[None, :] >= dropped[:, None]).astype(jnp.int32)
    offsets = jnp.concatenate([jnp.zeros((NB, 1), jnp.int32), nonzero[index]], axis=1)
    return ((rows[:, None] + offsets) % NB).astype(jnp.int32)


def levels(own_key, dims, split, low, high):
    gain = 1.0
    for position, shards_of in split:
        draws = jax.random.uniform(jax.random.fold_in(jax.random.fold_in(own_key, 6), position), (shards_of,), jnp.float32, low / len(split), high / len(split))
        gain = gain * jnp.repeat(jnp.exp(draws), dims[position] // shards_of).reshape((-1,) + (1,) * (len(dims) - 1 - position))
    return gain


def bell_draw(own_key, dims, deviation, reach, split=(), kind=jnp.bfloat16):
    values = jax.random.normal(own_key, dims, jnp.float32) * deviation
    if len(split) > 0:
        values = levels(own_key, dims, split, -0.22, 0.18) * values
    return jnp.clip(values, min=-reach, max=reach).astype(kind)


def setup_inputs(seed: int = 0) -> dict:
    arg_keys = jax.random.split(jax.random.key(seed), 3)
    density = bell_draw(arg_keys[0], (NB, K, BS, BS), (K * BS) ** -0.5, 0.15625, ((0, 256),), jnp.float32)
    pattern = draw_pattern(jax.random.fold_in(arg_keys[2], 71), 0)
    return dict(density=density, pattern=pattern)


def reference(density, pattern):
    def one_row(i):
        own = pattern[i]
        neighbor = pattern[own]
        equal = neighbor[:, None, :] == own[None, :, None]
        slot = jnp.argmax(equal.astype(jnp.int32), axis=2).astype(jnp.int32)
        valid = jnp.any(equal, axis=2).astype(jnp.float32)
        picked = density[own[:, None], slot] * valid[:, :, None, None]
        left = density[i]
        squared = jnp.einsum('sac,stcb->tab', left, picked, precision=lax.Precision.HIGHEST)
        rounded = lax.optimization_barrier(squared.astype(jnp.bfloat16)).astype(jnp.float32)
        cubed = jnp.einsum('sac,stcb->tab', rounded, picked, precision=lax.Precision.HIGHEST)
        return squared, 3.0 * squared - 2.0 * cubed

    squared, purified = lax.map(one_row, jnp.arange(NB, dtype=jnp.int32))
    return (squared, purified)
```

```python
import jax
import jax.numpy as jnp
from jax import lax
from jax.sharding import PartitionSpec as P

BAND = 3


def padded_2(value, sides, width):
    for axis, dim in sides:
        size, length = (lax.axis_size(axis), value.shape[dim])
        up = [(i, (i + 1) % size) for i in range(size)]
        down = [(j, i) for i, j in up]
        last = lax.slice_in_dim(value, length - width, length, axis=dim)
        initial = lax.slice_in_dim(value, 0, width, axis=dim)
        before = lax.ppermute(last, axis, up)
        after = lax.ppermute(initial, axis, down)
        value = jnp.concatenate([before, value, after], axis=dim)
    return value


def relay_pairs(mesh):
    devices = mesh.devices
    n_layer, n_blk = devices.shape
    try:
        where = {}
        for li in range(n_layer):
            for bi in range(n_blk):
                d = devices[li, bi]
                where[(tuple(d.coords), d.core_on_chip)] = (li, bi)
        depth = 1 + max(c[2] for c, _ in where)
        pairs = []
        for (coords, core), (li, bi) in where.items():
            x, y, z = coords
            step = 2 if core == 0 else -2
            one = where[((x, y, (z + step) % depth), core)]
            two = where[((x, y, (z + 2 * step) % depth), core)]
            if two != (li ^ 2, bi):
                return None
            pairs.append((li * n_blk + bi, one[0] * n_blk + one[1]))
        return sorted(pairs)
    except (AttributeError, KeyError, TypeError, IndexError):
        return None


def make_body(relay):
    def body(density, pattern):
        count_rows, slots, order, _ = density.shape
        n_layer = lax.axis_size("layer")
        width = order // n_layer
        me = lax.axis_index("layer")
        start_col = me * width
        total_rows = pattern.shape[0]
        first = lax.axis_index("blk") * count_rows
        own = lax.dynamic_slice_in_dim(pattern, first, count_rows, 0)
        neighbor = pattern[own]
        equal = neighbor[:, :, None, :] == own[:, None, :, None]
        slot = jnp.argmax(equal.astype(jnp.int32), axis=3)
        valid = jnp.any(equal, axis=3).astype(jnp.float32)
        row_ids = first + jnp.arange(count_rows, dtype=jnp.int32)
        offset = (own - row_ids[:, None] + BAND) % total_rows - BAND
        place = jnp.arange(count_rows, dtype=jnp.int32)[:, None] + BAND + offset
        col_part = lax.dynamic_slice_in_dim(density, start_col, width, 3)
        padded = padded_2(col_part, (("blk", 0),), BAND)
        highest = lax.Precision.HIGHEST
        picked = padded[place[:, :, None], slot] * valid[:, :, :, None, None]

        def product(left):
            return jnp.einsum("rsac,rstcb->rtab", left, picked, precision=highest)

        squared = product(density)
        rounded = squared.astype(jnp.bfloat16)
        across = [(i, i ^ 1) for i in range(n_layer)]
        mate = lax.ppermute(rounded, "layer", across)
        if relay is None:
            far = lax.ppermute(rounded, "layer", [(i, i ^ 2) for i in range(n_layer)])
        else:
            halfway = lax.ppermute(rounded, ("layer", "blk"), relay)
            far = lax.ppermute(halfway, ("layer", "blk"), relay)
        far_mate = lax.ppermute(far, "layer", across)
        pieces = jnp.stack([rounded, mate, far, far_mate])
        quarters = jnp.take(pieces, jnp.bitwise_xor(jnp.arange(4, dtype=jnp.int32), me), axis=0)
        gathered = jnp.moveaxis(quarters, 0, 3).reshape(count_rows, slots, order, order)
        cubed = product(gathered.astype(jnp.float32))
        return (squared, 3.0 * squared - 2.0 * cubed)

    return body


def solution(mesh):
    relay = relay_pairs(mesh) if mesh.shape["layer"] == 4 else None
    return jax.shard_map(
        make_body(relay),
        mesh=mesh,
        in_specs=(P("blk", None, None, None), P()),
        out_specs=(P("blk", None, None, "layer"), P("blk", None, None, "layer")),
        check_vma=False,
    )
```

```python
import jax
import jax.numpy as jnp
from jax import lax
from jax.sharding import PartitionSpec as P

BAND = 3


def padded_2(value, sides, width):
    for axis, dim in sides:
        size, length = (lax.axis_size(axis), value.shape[dim])
        up = [(i, (i + 1) % size) for i in range(size)]
        down = [(j, i) for i, j in up]
        last = lax.slice_in_dim(value, length - width, length, axis=dim)
        initial = lax.slice_in_dim(value, 0, width, axis=dim)
        before = lax.ppermute(last, axis, up)
        after = lax.ppermute(initial, axis, down)
        value = jnp.concatenate([before, value, after], axis=dim)
    return value


def relay_pairs(mesh):
    devices = mesh.devices
    n_layer, n_blk = devices.shape
    try:
        where = {}
        for li in range(n_layer):
            for bi in range(n_blk):
                d = devices[li, bi]
                where[(tuple(d.coords), d.core_on_chip)] = (li, bi)
        depth = 1 + max(c[2] for c, _ in where)
        pairs = []
        for (coords, core), (li, bi) in where.items():
            x, y, z = coords
            step = 2 if core == 0 else -2
            one = where[((x, y, (z + step) % depth), core)]
            two = where[((x, y, (z + 2 * step) % depth), core)]
            if two != (li ^ 2, bi):
                return None
            pairs.append((li * n_blk + bi, one[0] * n_blk + one[1]))
        return sorted(pairs)
    except (AttributeError, KeyError, TypeError, IndexError):
        return None


def make_body(relay):
    def body(density, pattern):
        count_rows, slots, order, _ = density.shape
        n_layer = lax.axis_size("layer")
        width = order // n_layer
        me = lax.axis_index("layer")
        start_col = me * width
        total_rows = pattern.shape[0]
        first = lax.axis_index("blk") * count_rows
        own = lax.dynamic_slice_in_dim(pattern, first, count_rows, 0)
        neighbor = pattern[own]
        equal = neighbor[:, :, None, :] == own[:, None, :, None]
        slot = jnp.argmax(equal.astype(jnp.int32), axis=3)
        valid = jnp.any(equal, axis=3).astype(jnp.float32)
        row_ids = first + jnp.arange(count_rows, dtype=jnp.int32)
        offset = (own - row_ids[:, None] + BAND) % total_rows - BAND
        place = jnp.arange(count_rows, dtype=jnp.int32)[:, None] + BAND + offset
        col_part = lax.dynamic_slice_in_dim(density, start_col, width, 3)
        padded = padded_2(col_part, (("blk", 0),), BAND)
        picked = padded[place[:, :, None], slot] * valid[:, :, :, None, None]
        squared = jnp.einsum("rsac,rstcb->rtab", density, picked, precision=lax.Precision.HIGH)
        rounded = squared.astype(jnp.bfloat16)
        high = picked.astype(jnp.bfloat16)
        low = (picked - high.astype(jnp.float32)).astype(jnp.bfloat16)

        def cubed_part(left, half):
            rows = lax.dynamic_slice_in_dim(high, half * 2 * width, 2 * width, 3)
            rest = lax.dynamic_slice_in_dim(low, half * 2 * width, 2 * width, 3)
            one = jnp.einsum("rsac,rstcb->rtab", left, rows, preferred_element_type=jnp.float32)
            two = jnp.einsum("rsac,rstcb->rtab", left, rest, preferred_element_type=jnp.float32)
            return one + two

        across = [(i, i ^ 1) for i in range(n_layer)]
        mate = lax.ppermute(rounded, "layer", across)
        even = (me % 2) == 0
        near_pair = jnp.where(even, jnp.concatenate([rounded, mate], 3), jnp.concatenate([mate, rounded], 3))
        near_part = cubed_part(near_pair, me // 2)
        if relay is None:
            far = lax.ppermute(rounded, "layer", [(i, i ^ 2) for i in range(n_layer)])
        else:
            halfway = lax.ppermute(rounded, ("layer", "blk"), relay)
            halfway, near_part = lax.optimization_barrier((halfway, near_part))
            far = lax.ppermute(halfway, ("layer", "blk"), relay)
        far_mate = lax.ppermute(far, "layer", across)
        far_pair = jnp.where(even, jnp.concatenate([far, far_mate], 3), jnp.concatenate([far_mate, far], 3))
        cubed = near_part + cubed_part(far_pair, 1 - me // 2)
        return (squared, 3.0 * squared - 2.0 * cubed)

    return body


def solution(mesh):
    relay = relay_pairs(mesh) if mesh.shape["layer"] == 4 else None
    return jax.shard_map(
        make_body(relay),
        mesh=mesh,
        in_specs=(P("blk", None, None, None), P()),
        out_specs=(P("blk", None, None, "layer"), P("blk", None, None, "layer")),
        check_vma=False,
    )
```

```python
import jax
import jax.numpy as jnp
from jax import lax
from jax.sharding import PartitionSpec as P

BAND = 3


def padded_2(value, sides, width):
    for axis, dim in sides:
        size, length = (lax.axis_size(axis), value.shape[dim])
        up = [(i, (i + 1) % size) for i in range(size)]
        down = [(j, i) for i, j in up]
        last = lax.slice_in_dim(value, length - width, length, axis=dim)
        initial = lax.slice_in_dim(value, 0, width, axis=dim)
        before = lax.ppermute(last, axis, up)
        after = lax.ppermute(initial, axis, down)
        value = jnp.concatenate([before, value, after], axis=dim)
    return value


def relay_pairs(mesh):
    devices = mesh.devices
    n_layer, n_blk = devices.shape
    try:
        where = {}
        for li in range(n_layer):
            for bi in range(n_blk):
                d = devices[li, bi]
                where[(tuple(d.coords), d.core_on_chip)] = (li, bi)
        depth = 1 + max(c[2] for c, _ in where)
        pairs = []
        for (coords, core), (li, bi) in where.items():
            x, y, z = coords
            step = 2 if core == 0 else -2
            one = where[((x, y, (z + step) % depth), core)]
            two = where[((x, y, (z + 2 * step) % depth), core)]
            if two != (li ^ 2, bi):
                return None
            pairs.append((li * n_blk + bi, one[0] * n_blk + one[1]))
        return sorted(pairs)
    except (AttributeError, KeyError, TypeError, IndexError):
        return None


def make_body(relay):
    def body(density, pattern):
        count_rows, slots, order, _ = density.shape
        n_layer = lax.axis_size("layer")
        width = order // n_layer
        me = lax.axis_index("layer")
        start_col = me * width
        total_rows = pattern.shape[0]
        first = lax.axis_index("blk") * count_rows
        own = lax.dynamic_slice_in_dim(pattern, first, count_rows, 0)
        neighbor = pattern[own]
        equal = neighbor[:, :, None, :] == own[:, None, :, None]
        slot = jnp.argmax(equal.astype(jnp.int32), axis=3)
        valid = jnp.any(equal, axis=3).astype(jnp.float32)
        row_ids = first + jnp.arange(count_rows, dtype=jnp.int32)
        offset = (own - row_ids[:, None] + BAND) % total_rows - BAND
        place = jnp.arange(count_rows, dtype=jnp.int32)[:, None] + BAND + offset
        col_part = lax.dynamic_slice_in_dim(density, start_col, width, 3)
        padded = padded_2(col_part, (("blk", 0),), BAND)
        picked = padded[place[:, :, None], slot] * valid[:, :, :, None, None]
        squared = jnp.einsum("rsac,rstcb->rtab", density, picked, precision=lax.Precision.HIGH)
        rounded = squared.astype(jnp.bfloat16)
        top = lax.reduce_precision(picked, exponent_bits=8, mantissa_bits=7)
        high = top.astype(jnp.bfloat16)
        low = (picked - top).astype(jnp.bfloat16)

        def cubed_part(left, half):
            rows = lax.dynamic_slice_in_dim(high, half * 2 * width, 2 * width, 3)
            rest = lax.dynamic_slice_in_dim(low, half * 2 * width, 2 * width, 3)
            one = jnp.einsum("rsac,rstcb->rtab", left, rows, preferred_element_type=jnp.float32)
            two = jnp.einsum("rsac,rstcb->rtab", left, rest, preferred_element_type=jnp.float32)
            return one + two

        across = [(i, i ^ 1) for i in range(n_layer)]
        mate = lax.ppermute(rounded, "layer", across)
        even = (me % 2) == 0
        near_pair = jnp.where(even, jnp.concatenate([rounded, mate], 3), jnp.concatenate([mate, rounded], 3))
        near_part = cubed_part(near_pair, me // 2)
        if relay is None:
            far = lax.ppermute(rounded, "layer", [(i, i ^ 2) for i in range(n_layer)])
        else:
            halfway = lax.ppermute(rounded, ("layer", "blk"), relay)
            halfway, near_part = lax.optimization_barrier((halfway, near_part))
            far = lax.ppermute(halfway, ("layer", "blk"), relay)
        far_mate = lax.ppermute(far, "layer", across)
        far_pair = jnp.where(even, jnp.concatenate([far, far_mate], 3), jnp.concatenate([far_mate, far], 3))
        cubed = near_part + cubed_part(far_pair, 1 - me // 2)
        return (squared, 3.0 * squared - 2.0 * cubed)

    return body


def solution(mesh):
    relay = relay_pairs(mesh) if mesh.shape["layer"] == 4 else None
    return jax.shard_map(
        make_body(relay),
        mesh=mesh,
        in_specs=(P("blk", None, None, None), P()),
        out_specs=(P("blk", None, None, "layer"), P("blk", None, None, "layer")),
        check_vma=False,
    )
```

```python
import jax
import jax.numpy as jnp
from jax import lax
from jax.sharding import PartitionSpec as P

BAND = 3


def padded_2(value, sides, width):
    for axis, dim in sides:
        size, length = (lax.axis_size(axis), value.shape[dim])
        up = [(i, (i + 1) % size) for i in range(size)]
        down = [(j, i) for i, j in up]
        last = lax.slice_in_dim(value, length - width, length, axis=dim)
        initial = lax.slice_in_dim(value, 0, width, axis=dim)
        before = lax.ppermute(last, axis, up)
        after = lax.ppermute(initial, axis, down)
        value = jnp.concatenate([before, value, after], axis=dim)
    return value


def relay_pairs(mesh):
    devices = mesh.devices
    n_layer, n_blk = devices.shape
    try:
        where = {}
        for li in range(n_layer):
            for bi in range(n_blk):
                d = devices[li, bi]
                where[(tuple(d.coords), d.core_on_chip)] = (li, bi)
        depth = 1 + max(c[2] for c, _ in where)
        pairs = []
        for (coords, core), (li, bi) in where.items():
            x, y, z = coords
            step = 2 if core == 0 else -2
            one = where[((x, y, (z + step) % depth), core)]
            two = where[((x, y, (z + 2 * step) % depth), core)]
            if two != (li ^ 2, bi):
                return None
            pairs.append((li * n_blk + bi, one[0] * n_blk + one[1]))
        return sorted(pairs)
    except (AttributeError, KeyError, TypeError, IndexError):
        return None


def make_body(relay):
    def body(density, pattern):
        count_rows, slots, order, _ = density.shape
        n_layer = lax.axis_size("layer")
        width = order // n_layer
        me = lax.axis_index("layer")
        start_col = me * width
        total_rows = pattern.shape[0]
        first = lax.axis_index("blk") * count_rows
        own = lax.dynamic_slice_in_dim(pattern, first, count_rows, 0)
        neighbor = pattern[own]
        equal = neighbor[:, :, None, :] == own[:, None, :, None]
        slot = jnp.argmax(equal.astype(jnp.int32), axis=3)
        valid = jnp.any(equal, axis=3).astype(jnp.float32)
        row_ids = first + jnp.arange(count_rows, dtype=jnp.int32)
        offset = (own - row_ids[:, None] + BAND) % total_rows - BAND
        place = jnp.arange(count_rows, dtype=jnp.int32)[:, None] + BAND + offset
        chunks = 2
        cw = width // chunks
        across = [(i, i ^ 1) for i in range(n_layer)]
        order_q = jnp.bitwise_xor(jnp.arange(4, dtype=jnp.int32), me)
        squares, lefts, pickeds = [], [], []
        arrived = None
        for h in range(chunks):
            col_part = lax.dynamic_slice_in_dim(density, start_col + h * cw, cw, 3)
            if arrived is not None:
                _, col_part = lax.optimization_barrier((arrived, col_part))
            padded = padded_2(col_part, (("blk", 0),), BAND)
            arrived = padded
            picked = padded[place[:, :, None], slot] * valid[:, :, :, None, None]
            squared = jnp.einsum("rsac,rstcb->rtab", density, picked, precision=lax.Precision.HIGH)
            rounded = squared.astype(jnp.bfloat16)
            mate = lax.ppermute(rounded, "layer", across)
            if relay is None:
                far = lax.ppermute(rounded, "layer", [(i, i ^ 2) for i in range(n_layer)])
            else:
                far = lax.ppermute(lax.ppermute(rounded, ("layer", "blk"), relay), ("layer", "blk"), relay)
            far_mate = lax.ppermute(far, "layer", across)
            pieces = jnp.take(jnp.stack([rounded, mate, far, far_mate]), order_q, axis=0)
            lefts.append(jnp.moveaxis(pieces, 0, 3).reshape(count_rows, slots, order, 4 * cw))
            squares.append(squared)
            pickeds.append(picked)
        squared = jnp.concatenate(squares, 3)
        picked = jnp.concatenate(pickeds, 4)
        top = lax.reduce_precision(picked, exponent_bits=8, mantissa_bits=7)
        high = top.astype(jnp.bfloat16)
        low = (picked - top).astype(jnp.bfloat16)
        grid = (count_rows, slots, slots, n_layer, chunks, cw, width)
        high = high.reshape(grid)
        low = low.reshape(grid)
        cubed = None
        for h in range(chunks):
            rows_high = high[:, :, :, :, h].reshape(count_rows, slots, slots, n_layer * cw, width)
            rows_low = low[:, :, :, :, h].reshape(count_rows, slots, slots, n_layer * cw, width)
            one = jnp.einsum("rsac,rstcb->rtab", lefts[h], rows_high, preferred_element_type=jnp.float32)
            two = jnp.einsum("rsac,rstcb->rtab", lefts[h], rows_low, preferred_element_type=jnp.float32)
            part = one + two
            cubed = part if cubed is None else cubed + part
        return (squared, 3.0 * squared - 2.0 * cubed)

    return body


def solution(mesh):
    relay = relay_pairs(mesh) if mesh.shape["layer"] == 4 else None
    return jax.shard_map(
        make_body(relay),
        mesh=mesh,
        in_specs=(P("blk", None, None, None), P()),
        out_specs=(P("blk", None, None, "layer"), P("blk", None, None, "layer")),
        check_vma=False,
    )
```

```python
import jax
import numpy as np
import jax.numpy as jnp
from jax import lax
from jax.sharding import PartitionSpec as P

BAND = 3


def padded_2(value, sides, width):
    for axis, dim in sides:
        size, length = (lax.axis_size(axis), value.shape[dim])
        up = [(i, (i + 1) % size) for i in range(size)]
        down = [(j, i) for i, j in up]
        last = lax.slice_in_dim(value, length - width, length, axis=dim)
        initial = lax.slice_in_dim(value, 0, width, axis=dim)
        before = lax.ppermute(last, axis, up)
        after = lax.ppermute(initial, axis, down)
        value = jnp.concatenate([before, value, after], axis=dim)
    return value


def relay_pairs(mesh):
    devices = mesh.devices
    n_layer, n_blk = devices.shape
    try:
        where = {}
        for li in range(n_layer):
            for bi in range(n_blk):
                d = devices[li, bi]
                where[(tuple(d.coords), d.core_on_chip)] = (li, bi)
        depth = 1 + max(c[2] for c, _ in where)
        pairs = []
        for (coords, core), (li, bi) in where.items():
            x, y, z = coords
            step = 2 if core == 0 else -2
            one = where[((x, y, (z + step) % depth), core)]
            two = where[((x, y, (z + 2 * step) % depth), core)]
            if two != (li ^ 2, bi):
                return None
            pairs.append((li * n_blk + bi, one[0] * n_blk + one[1]))
        return sorted(pairs)
    except (AttributeError, KeyError, TypeError, IndexError):
        return None


def make_body(relay):
    def body(density, pattern):
        count_rows, slots, order, _ = density.shape
        n_layer = lax.axis_size("layer")
        width = order // n_layer
        me = lax.axis_index("layer")
        start_col = me * width
        total_rows = pattern.shape[0]
        first = lax.axis_index("blk") * count_rows
        own = lax.dynamic_slice_in_dim(pattern, first, count_rows, 0)
        neighbor = pattern[own]
        equal = neighbor[:, :, None, :] == own[:, None, :, None]
        slot = jnp.argmax(equal.astype(jnp.int32), axis=3)
        valid = jnp.any(equal, axis=3).astype(jnp.float32)
        row_ids = first + jnp.arange(count_rows, dtype=jnp.int32)
        offset = (own - row_ids[:, None] + BAND) % total_rows - BAND
        place = jnp.arange(count_rows, dtype=jnp.int32)[:, None] + BAND + offset
        col_part = lax.dynamic_slice_in_dim(density, start_col, width, 3)
        m_ids = jnp.arange(count_rows, dtype=jnp.int32)
        groups = []
        for near in (True, False):
            lists = [[d for d in range(-BAND, BAND + 1) if (0 <= m + d < count_rows) == near] for m in range(count_rows)]
            size = max(len(ds) for ds in lists)
            offs = np.array([ds + [0] * (size - len(ds)) for ds in lists], np.int32)
            real = np.array([[1] * len(ds) + [0] * (size - len(ds)) for ds in lists], bool)
            groups.append((near, jnp.asarray(offs), jnp.asarray(real)))

        def offset_terms(near, offs, real, source):
            target = (row_ids[:, None] + offs) % total_rows
            hit = own[:, None, :] == target[:, :, None]
            present = jnp.logical_and(jnp.any(hit, axis=2), real)
            where_s = jnp.argmax(hit.astype(jnp.int32), axis=2)
            left = density[m_ids[:, None], where_s] * present[:, :, None, None].astype(jnp.float32)
            rows_of = pattern[target]
            match = rows_of[:, :, None, :] == own[:, None, :, None]
            use = jnp.logical_and(jnp.any(match, axis=3), present[:, :, None])
            where_u = jnp.argmax(match.astype(jnp.int32), axis=3)
            local = m_ids[:, None] + offs
            at = jnp.clip(local, 0, count_rows - 1) if near else local + BAND
            block = source[at[:, :, None], where_u] * use[:, :, :, None, None].astype(jnp.float32)
            return jnp.einsum("rsac,rstcb->rtab", left, block, precision=lax.Precision.HIGH)

        near_terms = offset_terms(groups[0][0], groups[0][1], groups[0][2], col_part)
        padded = padded_2(col_part, (("blk", 0),), BAND)
        squared = near_terms + offset_terms(groups[1][0], groups[1][1], groups[1][2], padded)
        picked = padded[place[:, :, None], slot] * valid[:, :, :, None, None]
        rounded = squared.astype(jnp.bfloat16)
        top = lax.reduce_precision(picked, exponent_bits=8, mantissa_bits=7)
        high = top.astype(jnp.bfloat16)
        low = (picked - top).astype(jnp.bfloat16)

        def cubed_part(left, half):
            rows = lax.dynamic_slice_in_dim(high, half * 2 * width, 2 * width, 3)
            rest = lax.dynamic_slice_in_dim(low, half * 2 * width, 2 * width, 3)
            one = jnp.einsum("rsac,rstcb->rtab", left, rows, preferred_element_type=jnp.float32)
            two = jnp.einsum("rsac,rstcb->rtab", left, rest, preferred_element_type=jnp.float32)
            return one + two

        across = [(i, i ^ 1) for i in range(n_layer)]
        mate = lax.ppermute(rounded, "layer", across)
        even = (me % 2) == 0
        near_pair = jnp.where(even, jnp.concatenate([rounded, mate], 3), jnp.concatenate([mate, rounded], 3))
        near_part = cubed_part(near_pair, me // 2)
        if relay is None:
            far = lax.ppermute(rounded, "layer", [(i, i ^ 2) for i in range(n_layer)])
        else:
            halfway = lax.ppermute(rounded, ("layer", "blk"), relay)
            halfway, near_part = lax.optimization_barrier((halfway, near_part))
            far = lax.ppermute(halfway, ("layer", "blk"), relay)
        far_mate = lax.ppermute(far, "layer", across)
        far_pair = jnp.where(even, jnp.concatenate([far, far_mate], 3), jnp.concatenate([far_mate, far], 3))
        cubed = near_part + cubed_part(far_pair, 1 - me // 2)
        return (squared, 3.0 * squared - 2.0 * cubed)

    return body


def solution(mesh):
    relay = relay_pairs(mesh) if mesh.shape["layer"] == 4 else None
    return jax.shard_map(
        make_body(relay),
        mesh=mesh,
        in_specs=(P("blk", None, None, None), P()),
        out_specs=(P("blk", None, None, "layer"), P("blk", None, None, "layer")),
        check_vma=False,
    )
```

```python
import jax
import jax.numpy as jnp
from jax import lax
from jax.sharding import PartitionSpec as P

BAND = 3


def padded_2(value, sides, width):
    for axis, dim in sides:
        size, length = (lax.axis_size(axis), value.shape[dim])
        up = [(i, (i + 1) % size) for i in range(size)]
        down = [(j, i) for i, j in up]
        last = lax.slice_in_dim(value, length - width, length, axis=dim)
        initial = lax.slice_in_dim(value, 0, width, axis=dim)
        before = lax.ppermute(last, axis, up)
        after = lax.ppermute(initial, axis, down)
        value = jnp.concatenate([before, value, after], axis=dim)
    return value


def relay_pairs(mesh):
    devices = mesh.devices
    n_layer, n_blk = devices.shape
    try:
        where = {}
        for li in range(n_layer):
            for bi in range(n_blk):
                d = devices[li, bi]
                where[(tuple(d.coords), d.core_on_chip)] = (li, bi)
        depth = 1 + max(c[2] for c, _ in where)
        pairs = []
        for (coords, core), (li, bi) in where.items():
            x, y, z = coords
            step = 2 if core == 0 else -2
            one = where[((x, y, (z + step) % depth), core)]
            two = where[((x, y, (z + 2 * step) % depth), core)]
            if two != (li ^ 2, bi):
                return None
            pairs.append((li * n_blk + bi, one[0] * n_blk + one[1]))
        return sorted(pairs)
    except (AttributeError, KeyError, TypeError, IndexError):
        return None


def make_body(relay):
    def body(density, pattern):
        count_rows, slots, order, _ = density.shape
        n_layer = lax.axis_size("layer")
        width = order // n_layer
        me = lax.axis_index("layer")
        start_col = me * width
        total_rows = pattern.shape[0]
        first = lax.axis_index("blk") * count_rows
        own = lax.dynamic_slice_in_dim(pattern, first, count_rows, 0)
        neighbor = pattern[own]
        equal = neighbor[:, :, None, :] == own[:, None, :, None]
        slot = jnp.argmax(equal.astype(jnp.int32), axis=3)
        valid = jnp.any(equal, axis=3).astype(jnp.float32)
        row_ids = first + jnp.arange(count_rows, dtype=jnp.int32)
        offset = (own - row_ids[:, None] + BAND) % total_rows - BAND
        place = jnp.arange(count_rows, dtype=jnp.int32)[:, None] + BAND + offset
        col_part = lax.dynamic_slice_in_dim(density, start_col, width, 3)
        padded = padded_2(col_part, (("blk", 0),), BAND)
        picked = padded[place[:, :, None], slot] * valid[:, :, :, None, None]
        squared = jnp.einsum("rsac,rstcb->rtab", density, picked, precision=lax.Precision.HIGH)
        rounded = squared.astype(jnp.bfloat16)
        top = lax.reduce_precision(picked, exponent_bits=8, mantissa_bits=7)
        high = top.astype(jnp.bfloat16)
        low = (picked - top).astype(jnp.bfloat16)

        def cubed_part(left, first, size):
            rows = lax.dynamic_slice_in_dim(high, first, size, 3)
            rest = lax.dynamic_slice_in_dim(low, first, size, 3)
            one = jnp.einsum("rsac,rstcb->rtab", left, rows, preferred_element_type=jnp.float32)
            two = jnp.einsum("rsac,rstcb->rtab", left, rest, preferred_element_type=jnp.float32)
            return one + two

        across = [(i, i ^ 1) for i in range(n_layer)]
        mate = lax.ppermute(rounded, "layer", across)
        even = (me % 2) == 0
        near_pair = jnp.where(even, jnp.concatenate([rounded, mate], 3), jnp.concatenate([mate, rounded], 3))
        near_part = cubed_part(near_pair, (me // 2) * 2 * width, 2 * width)
        if relay is None:
            far = lax.ppermute(rounded, "layer", [(i, i ^ 2) for i in range(n_layer)])
        else:
            halfway = lax.ppermute(rounded, ("layer", "blk"), relay)
            halfway, near_part = lax.optimization_barrier((halfway, near_part))
            far = lax.ppermute(halfway, ("layer", "blk"), relay)
        far_mate = lax.ppermute(far, "layer", across)
        far_part = cubed_part(far, (me ^ 2) * width, width)
        cubed = near_part + far_part + cubed_part(far_mate, (me ^ 3) * width, width)
        return (squared, 3.0 * squared - 2.0 * cubed)

    return body


def solution(mesh):
    relay = relay_pairs(mesh) if mesh.shape["layer"] == 4 else None
    return jax.shard_map(
        make_body(relay),
        mesh=mesh,
        in_specs=(P("blk", None, None, None), P()),
        out_specs=(P("blk", None, None, "layer"), P("blk", None, None, "layer")),
        check_vma=False,
    )
```

```python
import jax
import jax.numpy as jnp
from jax import lax
from jax.sharding import PartitionSpec as P

BAND = 3


def padded_2(value, sides, width):
    for axis, dim in sides:
        size, length = (lax.axis_size(axis), value.shape[dim])
        up = [(i, (i + 1) % size) for i in range(size)]
        down = [(j, i) for i, j in up]
        last = lax.slice_in_dim(value, length - width, length, axis=dim)
        initial = lax.slice_in_dim(value, 0, width, axis=dim)
        before = lax.ppermute(last, axis, up)
        after = lax.ppermute(initial, axis, down)
        value = jnp.concatenate([before, value, after], axis=dim)
    return value


def relay_pairs(mesh):
    devices = mesh.devices
    n_layer, n_blk = devices.shape
    try:
        where = {}
        for li in range(n_layer):
            for bi in range(n_blk):
                d = devices[li, bi]
                where[(tuple(d.coords), d.core_on_chip)] = (li, bi)
        depth = 1 + max(c[2] for c, _ in where)
        pairs = []
        for (coords, core), (li, bi) in where.items():
            x, y, z = coords
            step = 2 if core == 0 else -2
            one = where[((x, y, (z + step) % depth), core)]
            two = where[((x, y, (z + 2 * step) % depth), core)]
            if two != (li ^ 2, bi):
                return None
            pairs.append((li * n_blk + bi, one[0] * n_blk + one[1]))
        return sorted(pairs)
    except (AttributeError, KeyError, TypeError, IndexError):
        return None


def make_body(relay):
    def body(density, pattern):
        count_rows, slots, order, _ = density.shape
        n_layer = lax.axis_size("layer")
        width = order // n_layer
        me = lax.axis_index("layer")
        start_col = me * width
        total_rows = pattern.shape[0]
        first = lax.axis_index("blk") * count_rows
        own = lax.dynamic_slice_in_dim(pattern, first, count_rows, 0)
        neighbor = pattern[own]
        equal = neighbor[:, :, None, :] == own[:, None, :, None]
        slot = jnp.argmax(equal.astype(jnp.int32), axis=3)
        valid = jnp.any(equal, axis=3).astype(jnp.float32)
        row_ids = first + jnp.arange(count_rows, dtype=jnp.int32)
        offset = (own - row_ids[:, None] + BAND) % total_rows - BAND
        place = jnp.arange(count_rows, dtype=jnp.int32)[:, None] + BAND + offset
        col_part = lax.dynamic_slice_in_dim(density, start_col, width, 3)
        padded = padded_2(col_part, (("blk", 0),), BAND)
        across = [(i, i ^ 1) for i in range(n_layer)]
        even = (me % 2) == 0
        groups = [(0, 1), (1, count_rows)] if count_rows > 1 else [(0, count_rows)]
        squares, cubes = [], []
        for lo, hi in groups:
            picked = padded[place[lo:hi, :, None], slot[lo:hi]] * valid[lo:hi, :, :, None, None]
            squared = jnp.einsum("rsac,rstcb->rtab", density[lo:hi], picked, precision=lax.Precision.HIGH)
            rounded = squared.astype(jnp.bfloat16)
            top = lax.reduce_precision(picked, exponent_bits=8, mantissa_bits=7)
            high = top.astype(jnp.bfloat16)
            low = (picked - top).astype(jnp.bfloat16)

            def cubed_part(left, half):
                rows = lax.dynamic_slice_in_dim(high, half * 2 * width, 2 * width, 3)
                rest = lax.dynamic_slice_in_dim(low, half * 2 * width, 2 * width, 3)
                one = jnp.einsum("rsac,rstcb->rtab", left, rows, preferred_element_type=jnp.float32)
                two = jnp.einsum("rsac,rstcb->rtab", left, rest, preferred_element_type=jnp.float32)
                return one + two

            mate = lax.ppermute(rounded, "layer", across)
            near_pair = jnp.where(even, jnp.concatenate([rounded, mate], 3), jnp.concatenate([mate, rounded], 3))
            near_part = cubed_part(near_pair, me // 2)
            if relay is None:
                far = lax.ppermute(rounded, "layer", [(i, i ^ 2) for i in range(n_layer)])
            else:
                halfway = lax.ppermute(rounded, ("layer", "blk"), relay)
                halfway, near_part = lax.optimization_barrier((halfway, near_part))
                far = lax.ppermute(halfway, ("layer", "blk"), relay)
            far_mate = lax.ppermute(far, "layer", across)
            far_pair = jnp.where(even, jnp.concatenate([far, far_mate], 3), jnp.concatenate([far_mate, far], 3))
            squares.append(squared)
            cubes.append(near_part + cubed_part(far_pair, 1 - me // 2))
        squared = jnp.concatenate(squares, 0)
        cubed = jnp.concatenate(cubes, 0)
        return (squared, 3.0 * squared - 2.0 * cubed)

    return body


def solution(mesh):
    relay = relay_pairs(mesh) if mesh.shape["layer"] == 4 else None
    return jax.shard_map(
        make_body(relay),
        mesh=mesh,
        in_specs=(P("blk", None, None, None), P()),
        out_specs=(P("blk", None, None, "layer"), P("blk", None, None, "layer")),
        check_vma=False,
    )
```

```python
import jax
import jax.numpy as jnp
from jax import lax
from jax.sharding import PartitionSpec as P

BAND = 3


def padded_2(value, sides, width):
    for axis, dim in sides:
        size, length = (lax.axis_size(axis), value.shape[dim])
        up = [(i, (i + 1) % size) for i in range(size)]
        down = [(j, i) for i, j in up]
        last = lax.slice_in_dim(value, length - width, length, axis=dim)
        initial = lax.slice_in_dim(value, 0, width, axis=dim)
        before = lax.ppermute(last, axis, up)
        after = lax.ppermute(initial, axis, down)
        value = jnp.concatenate([before, value, after], axis=dim)
    return value


def relay_pairs(mesh):
    devices = mesh.devices
    n_layer, n_blk = devices.shape
    try:
        where = {}
        for li in range(n_layer):
            for bi in range(n_blk):
                d = devices[li, bi]
                where[(tuple(d.coords), d.core_on_chip)] = (li, bi)
        depth = 1 + max(c[2] for c, _ in where)
        pairs = []
        for (coords, core), (li, bi) in where.items():
            x, y, z = coords
            step = 2 if core == 0 else -2
            one = where[((x, y, (z + step) % depth), core)]
            two = where[((x, y, (z + 2 * step) % depth), core)]
            if two != (li ^ 2, bi):
                return None
            pairs.append((li * n_blk + bi, one[0] * n_blk + one[1]))
        return sorted(pairs)
    except (AttributeError, KeyError, TypeError, IndexError):
        return None


def make_body(relay):
    def body(density, pattern):
        count_rows, slots, order, _ = density.shape
        n_layer = lax.axis_size("layer")
        width = order // n_layer
        me = lax.axis_index("layer")
        start_col = me * width
        total_rows = pattern.shape[0]
        first = lax.axis_index("blk") * count_rows
        own = lax.dynamic_slice_in_dim(pattern, first, count_rows, 0)
        neighbor = pattern[own]
        equal = neighbor[:, :, None, :] == own[:, None, :, None]
        slot = jnp.argmax(equal.astype(jnp.int32), axis=3)
        valid = jnp.any(equal, axis=3).astype(jnp.float32)
        row_ids = first + jnp.arange(count_rows, dtype=jnp.int32)
        offset = (own - row_ids[:, None] + BAND) % total_rows - BAND
        place = jnp.arange(count_rows, dtype=jnp.int32)[:, None] + BAND + offset
        col_part = lax.dynamic_slice_in_dim(density, start_col, width, 3)
        padded = padded_2(col_part, (("blk", 0),), BAND)
        picked = padded[place[:, :, None], slot] * valid[:, :, :, None, None]
        squared = jnp.einsum("rsac,rstcb->rtab", density, picked, precision=lax.Precision.HIGH)
        rounded = squared.astype(jnp.bfloat16)
        top = lax.reduce_precision(picked, exponent_bits=8, mantissa_bits=7)
        high = top.astype(jnp.bfloat16)
        low = (picked - top).astype(jnp.bfloat16)

        def cubed_part(left, half):
            rows = lax.dynamic_slice_in_dim(high, half * 2 * width, 2 * width, 3)
            rest = lax.dynamic_slice_in_dim(low, half * 2 * width, 2 * width, 3)
            one = jnp.einsum("rsac,rstcb->rtab", left, rows, preferred_element_type=jnp.float32)
            two = jnp.einsum("rsac,rstcb->rtab", left, rest, preferred_element_type=jnp.float32)
            return one + two

        across = [(i, i ^ 1) for i in range(n_layer)]
        mate = lax.ppermute(rounded, "layer", across)
        even = (me % 2) == 0
        near_pair = jnp.where(even, jnp.concatenate([rounded, mate], 3), jnp.concatenate([mate, rounded], 3))
        near_part = cubed_part(near_pair, me // 2)
        if relay is None:
            far = lax.ppermute(rounded, "layer", [(i, i ^ 2) for i in range(n_layer)])
        else:
            halfway = lax.ppermute(rounded, ("layer", "blk"), relay)
            halfway, near_part = lax.optimization_barrier((halfway, near_part))
            far = lax.ppermute(halfway, ("layer", "blk"), relay)
        far_mate = lax.ppermute(far, "layer", across)
        far_pair = jnp.where(even, jnp.concatenate([far, far_mate], 3), jnp.concatenate([far_mate, far], 3))
        cubed = near_part + cubed_part(far_pair, 1 - me // 2)
        return (squared, 3.0 * squared - 2.0 * cubed)

    return body


def solution(mesh):
    relay = None
    return jax.shard_map(
        make_body(relay),
        mesh=mesh,
        in_specs=(P("blk", None, None, None), P()),
        out_specs=(P("blk", None, None, "layer"), P("blk", None, None, "layer")),
        check_vma=False,
    )
```

```python
import jax
import jax.numpy as jnp
from jax import lax
from jax.sharding import PartitionSpec as P

BAND = 3


def padded_2(value, sides, width):
    for axis, dim in sides:
        size, length = (lax.axis_size(axis), value.shape[dim])
        up = [(i, (i + 1) % size) for i in range(size)]
        down = [(j, i) for i, j in up]
        last = lax.slice_in_dim(value, length - width, length, axis=dim)
        initial = lax.slice_in_dim(value, 0, width, axis=dim)
        before = lax.ppermute(last, axis, up)
        after = lax.ppermute(initial, axis, down)
        value = jnp.concatenate([before, value, after], axis=dim)
    return value


def relay_pairs(mesh):
    devices = mesh.devices
    n_layer, n_blk = devices.shape
    try:
        where = {}
        for li in range(n_layer):
            for bi in range(n_blk):
                d = devices[li, bi]
                where[(tuple(d.coords), d.core_on_chip)] = (li, bi)
        depth = 1 + max(c[2] for c, _ in where)
        pairs = []
        for (coords, core), (li, bi) in where.items():
            x, y, z = coords
            step = 2 if core == 0 else -2
            one = where[((x, y, (z + step) % depth), core)]
            two = where[((x, y, (z + 2 * step) % depth), core)]
            if two != (li ^ 2, bi):
                return None
            pairs.append((li * n_blk + bi, one[0] * n_blk + one[1]))
        return sorted(pairs)
    except (AttributeError, KeyError, TypeError, IndexError):
        return None


def make_body(relay):
    def body(density, pattern):
        count_rows, slots, order, _ = density.shape
        n_layer = lax.axis_size("layer")
        width = order // n_layer
        me = lax.axis_index("layer")
        start_col = me * width
        total_rows = pattern.shape[0]
        first = lax.axis_index("blk") * count_rows
        own = lax.dynamic_slice_in_dim(pattern, first, count_rows, 0)
        neighbor = pattern[own]
        equal = neighbor[:, :, None, :] == own[:, None, :, None]
        slot = jnp.argmax(equal.astype(jnp.int32), axis=3)
        valid = jnp.any(equal, axis=3).astype(jnp.float32)
        row_ids = first + jnp.arange(count_rows, dtype=jnp.int32)
        offset = (own - row_ids[:, None] + BAND) % total_rows - BAND
        place = jnp.arange(count_rows, dtype=jnp.int32)[:, None] + BAND + offset
        col_part = lax.dynamic_slice_in_dim(density, start_col, width, 3)
        padded = padded_2(col_part, (("blk", 0),), BAND)
        picked = padded[place[:, :, None], slot] * valid[:, :, :, None, None]
        squared = jnp.einsum("rsac,rstcb->rtab", density, picked, precision=lax.Precision.HIGH)
        rounded = squared.astype(jnp.bfloat16)
        top = lax.reduce_precision(picked, exponent_bits=8, mantissa_bits=7)
        high = top.astype(jnp.bfloat16)
        low = (picked - top).astype(jnp.bfloat16)

        def cubed_part(left, half):
            rows = lax.dynamic_slice_in_dim(high, half * 2 * width, 2 * width, 3)
            rest = lax.dynamic_slice_in_dim(low, half * 2 * width, 2 * width, 3)
            one = jnp.einsum("rsac,rstcb->rtab", left, rows, preferred_element_type=jnp.float32)
            two = jnp.einsum("rsac,rstcb->rtab", left, rest, preferred_element_type=jnp.float32)
            return one + two

        across = [(i, i ^ 1) for i in range(n_layer)]
        mate = lax.ppermute(rounded, "layer", across)
        even = (me % 2) == 0
        near_pair = jnp.where(even, jnp.concatenate([rounded, mate], 3), jnp.concatenate([mate, rounded], 3))
        near_part = cubed_part(near_pair, me // 2)
        if relay is None:
            far = lax.ppermute(rounded, "layer", [(i, i ^ 2) for i in range(n_layer)])
            far, near_part = lax.optimization_barrier((far, near_part))
        else:
            halfway = lax.ppermute(rounded, ("layer", "blk"), relay)
            halfway, near_part = lax.optimization_barrier((halfway, near_part))
            far = lax.ppermute(halfway, ("layer", "blk"), relay)
        far_mate = lax.ppermute(far, "layer", across)
        far_pair = jnp.where(even, jnp.concatenate([far, far_mate], 3), jnp.concatenate([far_mate, far], 3))
        cubed = near_part + cubed_part(far_pair, 1 - me // 2)
        return (squared, 3.0 * squared - 2.0 * cubed)

    return body


def solution(mesh):
    relay = None
    return jax.shard_map(
        make_body(relay),
        mesh=mesh,
        in_specs=(P("blk", None, None, None), P()),
        out_specs=(P("blk", None, None, "layer"), P("blk", None, None, "layer")),
        check_vma=False,
    )
```
